512 devices in a mesh: rep: 32 (over x, z), tp: 16 (over y, core).
Axes of the slice: x: 4, y: 8, z: 8, core: 2. Of those that a mesh axis runs over, the one named last changes fastest.
Arguments:
- queries: bfloat16 [10240, 8192], P('rep', 'tp'), may hold values from -30 to 30
- fresh_kv: bfloat16 [10240, 4096], P('rep', 'tp'), may hold values from -6 to 6, as said below
- kv_cache: bfloat16 [1408, 16, 8, 256], P('rep', 'tp'), may hold values from -6 to 6, as said below
- cached_len: int32 [640], P('rep'), may hold values from 1 to 48, as said below
- page_table: int32 [640, 6], P('rep'), may hold values from 0 to 43, as said below
- out_weight: bfloat16 [8192, 4096], P('tp'), may hold values from -0.09375 to 0.09375
- adapter_down: bfloat16 [64, 64, 8192], P('rep', None, 'tp'), may hold values from -0.0625 to 0.0625
- pooled_up_weight: bfloat16 [64, 64, 4096], P('rep', None, 'tp'), may hold values from -0.75 to 0.75
- adapter_ids: int32 [640], P('rep'), may hold values from 0 to 63, as said below
- pool_slot: int32 [64], replicated, may hold values from 0 to 63, as said below
Outputs:
- adapted_output: bfloat16 [10240, 4096], P('rep', 'tp')
The draws below stay inside these ranges and needn't reach their ends.
Inputs may be any that keep to these rules, and one draw needn't show every extreme that they name: `kv_cache`: slots that hold the same key-value head are equal. `fresh_kv`: slots that hold the same key-value head are equal. `cached_len`: A row with cached length n uses its first ceil(n / 8) page table entries; in every replica some row has 48. `page_table`: entries index the 44 pages of the row's own replica. The pages that a row uses are distinct, no page is used by two rows of one replica, every page of a replica is used, and entries past a row's used pages repeat its first page. `adapter_ids`: row r of replica i is entry i * 20 + r. The owner of adapter a is replica pool_slot[a] // 2. Within one replica at most 2 rows name adapters of one owner, and one owner, the same for all replicas, is named by exactly 2 rows of every replica. A permutation: adapter a's blocks are adapter_down[pool_slot[a]] and pooled_up_weight[pool_slot[a]].
All inputs are finite; a program needn't handle non-finite values.
Results may differ from the reference program's by a relative error of at most 0.023.
Values may be sent and summed in bfloat16 or wider, within the bound.
No kernel may reach another device: no remote copies, remote signals or barrier semaphores. Data moves between devices by JAX's collectives and lax.ppermute only.
A program may use at most 64 MiB of HBM per device.

```python
import functools
import math
import jax
import jax.numpy as jnp
from jax import lax

HEADS = 64
KVH = 8
HD = 128
OUTPUT_FEATURES = 4096
RANK = 64
QUERY_TOKENS = 16
PAGE = 8
MAXP = 6
REPLICA_SEQS = 20
ADP_DEV = 2
KV_SLOTS = 16
NPAGES = 44
ADAPTERS = 64
N_REP = 32
N_TP = 16


def adapter_layout(key):
    base_key = jax.random.fold_in(key, 11)
    key_perm, key_hot, key_rows = jax.random.split(base_key, 3)
    adapter_count = ADP_DEV * N_REP
    slots = jax.random.permutation(key_perm, adapter_count).astype(jnp.int32)
    inverse = jnp.argsort(slots).astype(jnp.int32)
    row_cap = (REPLICA_SEQS + N_REP - 1) // N_REP + 1
    hot_owner = jax.random.randint(key_hot, (), 0, N_REP)

    def replica_rows(replica_key):
        key_rank, key_shuffle, key_local = jax.random.split(replica_key, 3)
        seat_count = N_REP * row_cap
        seat_ids = jnp.arange(seat_count)
        scoring = jax.random.permutation(key_rank, seat_count)
        scoring = jnp.where(seat_ids // row_cap == hot_owner, seat_ids % row_cap - seat_count, scoring)
        ranking = jnp.argsort(scoring)
        chosen = ranking[:REPLICA_SEQS]
        chosen = chosen[jax.random.permutation(key_shuffle, REPLICA_SEQS)]
        owners = chosen // row_cap
        local_pick = jax.random.randint(key_local, (REPLICA_SEQS,), 0, ADP_DEV)
        return inverse[owners * ADP_DEV + local_pick]
    replica_keys = jax.random.split(key_rows, N_REP)
    named = jax.vmap(replica_rows)(replica_keys).reshape(N_REP * REPLICA_SEQS)
    return (slots, named.astype(jnp.int32))


def page_layout(key):
    base_key = jax.random.fold_in(key, 23)

    def replica_pages(replica_key):
        key_taken, key_shuffle, key_order, key_fill = jax.random.split(replica_key, 4)
        extra_pages = NPAGES - REPLICA_SEQS - (MAXP - 1)
        spare_slots = (REPLICA_SEQS - 1) * (MAXP - 1)
        taken_slots = (jax.random.permutation(key_taken, spare_slots) < extra_pages).astype(jnp.int32)
        counts_rest = 1 + jnp.sum(taken_slots.reshape(REPLICA_SEQS - 1, MAXP - 1), axis=1)
        counts = jnp.concatenate([jnp.full((1,), MAXP, jnp.int32), counts_rest.astype(jnp.int32)])
        shuffle = jax.random.permutation(key_shuffle, REPLICA_SEQS)
        counts = counts[shuffle]
        first_page = jnp.cumsum(counts) - counts
        page_order = jax.random.permutation(key_order, NPAGES).astype(jnp.int32)
        column = jnp.arange(MAXP)[None, :]
        offset = first_page[:, None] + jnp.where(column < counts[:, None], column, 0)
        page_rows = page_order[offset]
        last_fill = jax.random.randint(key_fill, (REPLICA_SEQS,), 1, PAGE + 1)
        last_fill = jnp.where(shuffle == 0, PAGE, last_fill)
        length = (counts - 1) * PAGE + last_fill
        return (page_rows.astype(jnp.int32), length.astype(jnp.int32))
    replica_keys = jax.random.split(base_key, N_REP)
    tables, lengths = jax.vmap(replica_pages)(replica_keys)
    return (tables.reshape(N_REP * REPLICA_SEQS, MAXP), lengths.reshape(N_REP * REPLICA_SEQS))


def draw_pool_slot(key, part):
    return adapter_layout(key)[0]


def draw_adapter_ids(key, part):
    return adapter_layout(key)[1]


def draw_page_table(key, part):
    return page_layout(key)[0]


def draw_cached_len(key, part):
    return page_layout(key)[1]


def draw_queries(key, part):
    full_shape = (N_REP * REPLICA_SEQS * QUERY_TOKENS, HEADS * HD)
    key_noise = jax.random.fold_in(key, 0)
    values = jnp.clip(jax.random.normal(key_noise, full_shape, jnp.float32), -6.0, 6.0)
    return values.astype(jnp.bfloat16)


def draw_fresh_kv(key, part):
    base_shape = (N_REP * REPLICA_SEQS * QUERY_TOKENS, KVH, 2 * HD)
    values = jnp.clip(jax.random.normal(key, base_shape, jnp.float32), -6.0, 6.0)
    values = jnp.repeat(values, KV_SLOTS // KVH, axis=1)
    return values.reshape(N_REP * REPLICA_SEQS * QUERY_TOKENS, KV_SLOTS * 2 * HD).astype(jnp.bfloat16)


def draw_kv_cache(key, part):
    base_shape = (N_REP * NPAGES, KVH, PAGE, 2 * HD)
    values = jnp.clip(jax.random.normal(key, base_shape, jnp.float32), -6.0, 6.0)
    values = jnp.repeat(values, KV_SLOTS // KVH, axis=1)
    return values.astype(jnp.bfloat16)


def with_spikes(values, own_key, source, target, shards_of, factor):
    def block_of(dim):
        return (jnp.arange(values.shape[dim]) // (values.shape[dim] // shards_of)).reshape((-1,) + (1,) * (values.ndim - 1 - dim))

    near = jax.random.permutation(own_key, shards_of)[block_of(target)]
    second = (block_of(target) + shards_of // 2) % shards_of
    return jnp.where((block_of(source) == near) | (block_of(source) == second), factor * values, values)


def block_scale(stream_key, shape, pieces, low, top_value):
    level, own = 1.0, jax.random.fold_in(stream_key, 6)
    for dim, parts in pieces:
        steps = jnp.exp(jax.random.uniform(jax.random.fold_in(own, dim), (parts,), jnp.float32, low / len(pieces), top_value / len(pieces)))
        level = level * jnp.repeat(steps, shape[dim] // parts).reshape([-1 if axis == dim else 1 for axis in range(len(shape))])
    return level


def centred(own_key, dims, deviation, most, cuts=(), dtype=jnp.bfloat16):
    array = deviation * jax.random.normal(own_key, dims, jnp.float32)
    if cuts:
        array = array * block_scale(own_key, dims, cuts, -0.22, 0.18)
    return jnp.clip(array, -most, most).astype(dtype)


def heavy_noise(key, dims, deviation, reach, cuts, heavy, dtype=jnp.bfloat16):
    values = deviation * jax.random.normal(key, dims, jnp.float32)
    if cuts:
        values = values * block_scale(key, dims, cuts, -0.22, 0.18)
    return jnp.clip(with_spikes(values, jax.random.fold_in(key, 3), *heavy), -reach, reach).astype(dtype)


def setup_inputs(seed: int = 0) -> dict:
    keys = jax.random.split(jax.random.key(seed), 11)
    queries = draw_queries(jax.random.fold_in(keys[10], 71), 0)
    fresh_kv = draw_fresh_kv(jax.random.fold_in(keys[10], 71), 0)
    kv_cache = draw_kv_cache(jax.random.fold_in(keys[10], 71), 0)
    cached_len = draw_cached_len(jax.random.fold_in(keys[10], 71), 0)
    page_table = draw_page_table(jax.random.fold_in(keys[10], 71), 0)
    out_weight = heavy_noise(keys[5], (HEADS * HD, OUTPUT_FEATURES), (HEADS * HD) ** -0.5, 0.09375, ((0, 16),), (0, 1, 16, 2.0))
    adapter_down = centred(keys[6], (ADAPTERS, RANK, HEADS * HD), (HEADS * HD) ** -0.5, 0.0625, ((0, 32), (2, 16)))
    pooled_up_weight = centred(keys[7], (ADAPTERS, RANK, OUTPUT_FEATURES), RANK ** -0.5, 0.75, ((0, 32), (2, 16)))
    adapter_ids = draw_adapter_ids(jax.random.fold_in(keys[10], 71), 0)
    pool_slot = draw_pool_slot(jax.random.fold_in(keys[10], 71), 0)
    return dict(queries=queries, fresh_kv=fresh_kv, kv_cache=kv_cache, cached_len=cached_len, page_table=page_table, out_weight=out_weight, adapter_down=adapter_down, pooled_up_weight=pooled_up_weight, adapter_ids=adapter_ids, pool_slot=pool_slot)


ADAPTER_SCALE = 2.0

def attend(queries, fresh_rows, cache_rows, lengths, pages_of):
    feat_width = HEADS * HD
    group_size = HEADS // KV_SLOTS
    cache_span = MAXP * PAGE
    query_five = queries.reshape(REPLICA_SEQS, QUERY_TOKENS, KV_SLOTS, group_size, HD).astype(jnp.float32)
    paged_kv = cache_rows[pages_of]
    paged_kv = paged_kv.transpose(0, 2, 1, 3, 4).reshape(REPLICA_SEQS, KV_SLOTS, cache_span, 2 * HD)
    recent = fresh_rows.reshape(REPLICA_SEQS, QUERY_TOKENS, KV_SLOTS, 2 * HD).transpose(0, 2, 1, 3)
    entries = jnp.concatenate([paged_kv, recent], axis=2).astype(jnp.float32)
    key_part = entries[..., :HD]
    value_part = entries[..., HD:]
    scores = jnp.einsum('rqghd,rgkd->rghqk', query_five, key_part, precision=lax.Precision.HIGHEST) / math.sqrt(HD)
    entry_ids = jnp.arange(cache_span + QUERY_TOKENS)[None, None, :]
    token_ids = jnp.arange(QUERY_TOKENS)[None, :, None]
    allowed = jnp.where(entry_ids < cache_span, entry_ids < lengths[:, None, None], entry_ids - cache_span <= token_ids)
    scores = jnp.where(allowed[:, None, None, :, :], scores, -jnp.inf)
    peak_score = lax.optimization_barrier(jnp.max(scores, axis=-1, keepdims=True))
    raised = jnp.exp(scores - peak_score)
    weights = (raised / lax.optimization_barrier(jnp.sum(raised, axis=-1, keepdims=True))).astype(jnp.bfloat16)
    heads_out = jnp.einsum('rghqk,rgkd->rqghd', weights.astype(jnp.float32), value_part, precision=lax.Precision.HIGHEST)
    return heads_out.reshape(REPLICA_SEQS * QUERY_TOKENS, feat_width).astype(jnp.bfloat16)

def replica_layer(operand_set, out_weight, adapter_down, pooled_up_weight, pool_slot):
    queries, fresh_rows, cache_rows, lengths, pages_of, adapter_ids = operand_set
    feat_width = HEADS * HD
    attended = attend(queries, fresh_rows, cache_rows, lengths, pages_of)
    split_in = attended.reshape(REPLICA_SEQS * QUERY_TOKENS, N_TP, feat_width // N_TP).astype(jnp.float32)
    split_weight = out_weight.reshape(N_TP, feat_width // N_TP, OUTPUT_FEATURES).astype(jnp.float32)
    partial_sums = jnp.einsum('tgf,gfd->gtd', split_in, split_weight, precision=lax.Precision.HIGHEST)
    partial_sums = lax.optimization_barrier(partial_sums.astype(jnp.bfloat16))
    plain_output = lax.optimization_barrier(jnp.sum(partial_sums.astype(jnp.float32), axis=0))
    pool_position = pool_slot[adapter_ids]
    by_row = attended.reshape(REPLICA_SEQS, QUERY_TOKENS, feat_width).astype(jnp.float32)
    down_projected = jnp.einsum('rqf,rkf->rqk', by_row, adapter_down[pool_position].astype(jnp.float32), precision=lax.Precision.HIGHEST).astype(jnp.bfloat16)
    adapter_correction = jnp.einsum('owe,oet->owt', down_projected.astype(jnp.float32), pooled_up_weight[pool_position].astype(jnp.float32), precision=lax.Precision.HIGHEST).astype(jnp.bfloat16)
    adapted_output = plain_output + ADAPTER_SCALE * adapter_correction.reshape(REPLICA_SEQS * QUERY_TOKENS, OUTPUT_FEATURES).astype(jnp.float32)
    return adapted_output.astype(jnp.bfloat16)

def reference(queries, fresh_kv, kv_cache, cached_len, page_table, out_weight, adapter_down, pooled_up_weight, adapter_ids, pool_slot):
    token_count = REPLICA_SEQS * QUERY_TOKENS
    operand_set = (queries.reshape(N_REP, token_count, HEADS * HD), fresh_kv.reshape(N_REP, token_count, KV_SLOTS * 2 * HD), kv_cache.reshape(N_REP, NPAGES, KV_SLOTS, PAGE, 2 * HD), cached_len.reshape(N_REP, REPLICA_SEQS), page_table.reshape(N_REP, REPLICA_SEQS, MAXP), adapter_ids.reshape(N_REP, REPLICA_SEQS))
    layer_fn = functools.partial(replica_layer, out_weight=out_weight, adapter_down=adapter_down, pooled_up_weight=pooled_up_weight, pool_slot=pool_slot)
    layered = lax.map(layer_fn, operand_set)
    return layered.reshape(N_REP * token_count, OUTPUT_FEATURES)
```

```python
import math

import jax
import jax.numpy as jnp
from jax import lax
from jax.sharding import PartitionSpec as P

ADAPTER_SCALE = 2.0


def shards(
    queries,
    fresh_kv,
    kv_cache,
    cached_len,
    page_table,
    out_weight,
    adapter_down,
    pooled_up_weight,
    adapter_ids,
    pool_slot,
):
    row_count = cached_len.shape[0]
    token_count = queries.shape[0]
    per_row = token_count // row_count
    slot_count = kv_cache.shape[1]
    page_len = kv_cache.shape[2]
    head_dim = kv_cache.shape[3] // 2
    feat_width = queries.shape[1]
    head_count = feat_width // head_dim
    heads_per_slot = head_count // slot_count
    cache_span = page_table.shape[1] * page_len
    output_columns = pooled_up_weight.shape[2]
    paged_kv = (
        kv_cache[page_table]
        .transpose(0, 2, 1, 3, 4)
        .reshape(row_count, slot_count, cache_span, 2 * head_dim)
    )
    recent = fresh_kv.reshape(row_count, per_row, slot_count, 2 * head_dim).transpose(0, 2, 1, 3)
    entries = jnp.concatenate([paged_kv, recent], axis=2)
    key_part = entries[..., :head_dim]
    value_part = entries[..., head_dim:]
    query_rows = queries.reshape(
        row_count, per_row, slot_count, heads_per_slot, head_dim
    ).transpose(0, 2, 1, 3, 4)
    query_rows = query_rows.reshape(row_count, slot_count, per_row * heads_per_slot, head_dim)
    scores = jnp.einsum(
        "rsad,rskd->rsak", query_rows, key_part, preferred_element_type=jnp.float32
    ) / math.sqrt(head_dim)
    entry_ids = jnp.arange(cache_span + per_row)[None, None, None, :]
    token_ids = (jnp.arange(per_row * heads_per_slot) // heads_per_slot)[None, None, :, None]
    allowed = jnp.where(
        entry_ids < cache_span,
        entry_ids < cached_len[:, None, None, None],
        entry_ids - cache_span <= token_ids,
    )
    scores = jnp.where(allowed, scores, -jnp.inf)
    peak_score = jnp.max(scores, axis=-1, keepdims=True)
    raised = jnp.exp(scores - peak_score)
    weights = (raised / jnp.sum(raised, axis=-1, keepdims=True)).astype(jnp.bfloat16)
    attended = jnp.einsum(
        "rsak,rskd->rsad", weights, value_part, preferred_element_type=jnp.float32
    ).astype(jnp.bfloat16)
    attended = attended.reshape(row_count, slot_count, per_row, heads_per_slot, head_dim).transpose(
        0, 2, 1, 3, 4
    )
    attended = attended.reshape(token_count, feat_width)
    plain_output = (
        lax.psum_scatter(
            lax.dot_general(
                out_weight, attended, (((0,), (1,)), ((), ())), preferred_element_type=jnp.float32
            ).astype(jnp.bfloat16),
            "tp",
            scatter_dimension=0,
            tiled=True,
        )
        .astype(jnp.float32)
        .T
    )
    slot_hits = adapter_ids[:, None] == jnp.arange(pool_slot.shape[0])[None, :]
    pool_position = jnp.sum(jnp.where(slot_hits, pool_slot[None, :], 0), axis=1)
    replicas = lax.axis_size("rep")
    local_count = adapter_down.shape[0]
    capacity = (row_count + replicas - 1) // replicas + 1
    owner_of = pool_position // local_count
    local_slot = pool_position % local_count
    same_owner = owner_of[:, None] == owner_of[None, :]
    earlier = jnp.arange(row_count)[None, :] < jnp.arange(row_count)[:, None]
    seat_of = jnp.sum(same_owner & earlier, axis=1)
    target = owner_of * capacity + seat_of
    placing = jnp.arange(replicas * capacity)[:, None] == target[None, :]
    placing_mat = placing.astype(jnp.bfloat16)
    by_row = attended.reshape(row_count, per_row, feat_width)
    send_rows = jnp.einsum(
        "sr,rqf->sqf", placing_mat, by_row, preferred_element_type=jnp.float32
    ).astype(jnp.bfloat16)
    seat_slot = jnp.sum(jnp.where(placing, local_slot[None, :], 0), axis=1).astype(jnp.bfloat16)
    marker = jnp.broadcast_to(seat_slot[:, None, None], (replicas * capacity, 1, feat_width))
    payload = jnp.concatenate([send_rows, marker], axis=1).reshape(
        replicas, capacity, per_row + 1, feat_width
    )
    arrived = lax.all_to_all(payload, "rep", split_axis=0, concat_axis=0, tiled=True)
    arrived = arrived.reshape(replicas * capacity, per_row + 1, feat_width)
    seat_rows = arrived[:, :per_row, :]
    wants_one = arrived[:, per_row, 0] > 0.5
    shrink_both = jnp.einsum(
        "sqf,jkf->jsqk", seat_rows, adapter_down, preferred_element_type=jnp.float32
    )
    shrink_part = jnp.where(wants_one[:, None, None], shrink_both[1], shrink_both[0])
    down_projected = lax.psum(shrink_part.astype(jnp.bfloat16), "tp")
    up_both = jnp.einsum(
        "sqk,jkd->jsqd", down_projected, pooled_up_weight, preferred_element_type=jnp.float32
    )
    seat_delta = jnp.where(wants_one[:, None, None], up_both[1], up_both[0]).astype(jnp.bfloat16)
    returned = lax.all_to_all(
        seat_delta.reshape(replicas, capacity, per_row, output_columns),
        "rep",
        split_axis=0,
        concat_axis=0,
        tiled=True,
    ).reshape(replicas * capacity, per_row, output_columns)
    adapter_correction = jnp.einsum(
        "sr,sqd->rqd", placing_mat, returned, preferred_element_type=jnp.float32
    )
    adapted_output = plain_output + ADAPTER_SCALE * adapter_correction.reshape(
        token_count, output_columns
    )
    return adapted_output.astype(jnp.bfloat16)


def solution(mesh):
    return jax.shard_map(
        shards,
        mesh=mesh,
        in_specs=(
            P("rep", "tp"),
            P("rep", "tp"),
            P("rep", "tp", None, None),
            P("rep"),
            P("rep", None),
            P("tp", None),
            P("rep", None, "tp"),
            P("rep", None, "tp"),
            P("rep"),
            P(),
        ),
        out_specs=P("rep", "tp"),
        check_vma=False,
    )
```

```python
import math

import jax
import jax.numpy as jnp
from jax import lax
from jax.sharding import PartitionSpec as P

ADAPTER_SCALE = 2.0


def tp_sum(part):
    width = lax.axis_size("tp")
    chunks = part.reshape(width, -1)
    gathered = lax.all_to_all(chunks, "tp", split_axis=0, concat_axis=0, tiled=True)
    summed = jnp.sum(gathered.astype(jnp.float32), axis=0, keepdims=True).astype(jnp.bfloat16)
    spread = lax.all_to_all(
        jnp.broadcast_to(summed, chunks.shape), "tp", split_axis=0, concat_axis=0, tiled=True
    )
    return spread.reshape(part.shape)


def shards(
    queries,
    fresh_kv,
    kv_cache,
    cached_len,
    page_table,
    out_weight,
    adapter_down,
    pooled_up_weight,
    adapter_ids,
    pool_slot,
):
    row_count = cached_len.shape[0]
    token_count = queries.shape[0]
    per_row = token_count // row_count
    slot_count = kv_cache.shape[1]
    page_len = kv_cache.shape[2]
    head_dim = kv_cache.shape[3] // 2
    feat_width = queries.shape[1]
    head_count = feat_width // head_dim
    heads_per_slot = head_count // slot_count
    cache_span = page_table.shape[1] * page_len
    output_columns = pooled_up_weight.shape[2]
    paged_kv = (
        kv_cache[page_table]
        .transpose(0, 2, 1, 3, 4)
        .reshape(row_count, slot_count, cache_span, 2 * head_dim)
    )
    recent = fresh_kv.reshape(row_count, per_row, slot_count, 2 * head_dim).transpose(0, 2, 1, 3)
    entries = jnp.concatenate([paged_kv, recent], axis=2)
    key_part = entries[..., :head_dim]
    value_part = entries[..., head_dim:]
    query_rows = queries.reshape(
        row_count, per_row, slot_count, heads_per_slot, head_dim
    ).transpose(0, 2, 1, 3, 4)
    query_rows = query_rows.reshape(row_count, slot_count, per_row * heads_per_slot, head_dim)
    scores = jnp.einsum(
        "rsad,rskd->rsak", query_rows, key_part, preferred_element_type=jnp.float32
    ) / math.sqrt(head_dim)
    entry_ids = jnp.arange(cache_span + per_row)[None, None, None, :]
    token_ids = (jnp.arange(per_row * heads_per_slot) // heads_per_slot)[None, None, :, None]
    allowed = jnp.where(
        entry_ids < cache_span,
        entry_ids < cached_len[:, None, None, None],
        entry_ids - cache_span <= token_ids,
    )
    scores = jnp.where(allowed, scores, -jnp.inf)
    peak_score = jnp.max(scores, axis=-1, keepdims=True)
    raised = jnp.exp(scores - peak_score)
    weights = (raised / jnp.sum(raised, axis=-1, keepdims=True)).astype(jnp.bfloat16)
    attended = jnp.einsum(
        "rsak,rskd->rsad", weights, value_part, preferred_element_type=jnp.float32
    ).astype(jnp.bfloat16)
    attended = attended.reshape(row_count, slot_count, per_row, heads_per_slot, head_dim).transpose(
        0, 2, 1, 3, 4
    )
    attended = attended.reshape(token_count, feat_width)
    plain_output = (
        lax.psum_scatter(
            lax.dot_general(
                out_weight, attended, (((0,), (1,)), ((), ())), preferred_element_type=jnp.float32
            ).astype(jnp.bfloat16),
            "tp",
            scatter_dimension=0,
            tiled=True,
        )
        .astype(jnp.float32)
        .T
    )
    slot_hits = adapter_ids[:, None] == jnp.arange(pool_slot.shape[0])[None, :]
    pool_position = jnp.sum(jnp.where(slot_hits, pool_slot[None, :], 0), axis=1)
    replicas = lax.axis_size("rep")
    local_count = adapter_down.shape[0]
    capacity = (row_count + replicas - 1) // replicas + 1
    owner_of = pool_position // local_count
    local_slot = pool_position % local_count
    same_owner = owner_of[:, None] == owner_of[None, :]
    earlier = jnp.arange(row_count)[None, :] < jnp.arange(row_count)[:, None]
    seat_of = jnp.sum(same_owner & earlier, axis=1)
    target = owner_of * capacity + seat_of
    placing = jnp.arange(replicas * capacity)[:, None] == target[None, :]
    placing_mat = placing.astype(jnp.bfloat16)
    by_row = attended.reshape(row_count, per_row, feat_width)
    send_rows = jnp.einsum(
        "sr,rqf->sqf", placing_mat, by_row, preferred_element_type=jnp.float32
    ).astype(jnp.bfloat16)
    seat_slot = jnp.sum(jnp.where(placing, local_slot[None, :], 0), axis=1).astype(jnp.bfloat16)
    marker = jnp.broadcast_to(seat_slot[:, None, None], (replicas * capacity, 1, feat_width))
    payload = jnp.concatenate([send_rows, marker], axis=1).reshape(
        replicas, capacity, per_row + 1, feat_width
    )
    arrived = lax.all_to_all(payload, "rep", split_axis=0, concat_axis=0, tiled=True)
    arrived = arrived.reshape(replicas * capacity, per_row + 1, feat_width)
    seat_rows = arrived[:, :per_row, :]
    wants_one = arrived[:, per_row, 0] > 0.5
    shrink_both = jnp.einsum(
        "sqf,jkf->jsqk", seat_rows, adapter_down, preferred_element_type=jnp.float32
    )
    shrink_part = jnp.where(wants_one[:, None, None], shrink_both[1], shrink_both[0])
    down_projected = tp_sum(shrink_part.astype(jnp.bfloat16))
    up_both = jnp.einsum(
        "sqk,jkd->jsqd", down_projected, pooled_up_weight, preferred_element_type=jnp.float32
    )
    seat_delta = jnp.where(wants_one[:, None, None], up_both[1], up_both[0]).astype(jnp.bfloat16)
    returned = lax.all_to_all(
        seat_delta.reshape(replicas, capacity, per_row, output_columns),
        "rep",
        split_axis=0,
        concat_axis=0,
        tiled=True,
    ).reshape(replicas * capacity, per_row, output_columns)
    adapter_correction = jnp.einsum(
        "sr,sqd->rqd", placing_mat, returned, preferred_element_type=jnp.float32
    )
    adapted_output = plain_output + ADAPTER_SCALE * adapter_correction.reshape(
        token_count, output_columns
    )
    return adapted_output.astype(jnp.bfloat16)


def solution(mesh):
    return jax.shard_map(
        shards,
        mesh=mesh,
        in_specs=(
            P("rep", "tp"),
            P("rep", "tp"),
            P("rep", "tp", None, None),
            P("rep"),
            P("rep", None),
            P("tp", None),
            P("rep", None, "tp"),
            P("rep", None, "tp"),
            P("rep"),
            P(),
        ),
        out_specs=P("rep", "tp"),
        check_vma=False,
    )
```

```python
import math

import jax
import jax.numpy as jnp
from jax import lax
from jax.sharding import PartitionSpec as P

ADAPTER_SCALE = 2.0


def tp_sum(part):
    width = lax.axis_size("tp")
    chunks = part.reshape(width, -1)
    gathered = lax.all_to_all(chunks, "tp", split_axis=0, concat_axis=0, tiled=True)
    summed = jnp.sum(gathered.astype(jnp.float32), axis=0, keepdims=True).astype(jnp.bfloat16)
    spread = lax.all_to_all(
        jnp.broadcast_to(summed, chunks.shape), "tp", split_axis=0, concat_axis=0, tiled=True
    )
    return spread.reshape(part.shape)


def shards(
    queries,
    fresh_kv,
    kv_cache,
    cached_len,
    page_table,
    out_weight,
    adapter_down,
    pooled_up_weight,
    adapter_ids,
    pool_slot,
):
    row_count = cached_len.shape[0]
    token_count = queries.shape[0]
    per_row = token_count // row_count
    slot_count = kv_cache.shape[1]
    page_len = kv_cache.shape[2]
    head_dim = kv_cache.shape[3] // 2
    feat_width = queries.shape[1]
    head_count = feat_width // head_dim
    heads_per_slot = head_count // slot_count
    cache_span = page_table.shape[1] * page_len
    output_columns = pooled_up_weight.shape[2]
    paged_kv = (
        kv_cache[page_table]
        .transpose(0, 2, 1, 3, 4)
        .reshape(row_count, slot_count, cache_span, 2 * head_dim)
    )
    recent = fresh_kv.reshape(row_count, per_row, slot_count, 2 * head_dim).transpose(0, 2, 1, 3)
    entries = jnp.concatenate([paged_kv, recent], axis=2)
    key_part = entries[..., :head_dim]
    value_part = entries[..., head_dim:]
    query_rows = queries.reshape(
        row_count, per_row, slot_count, heads_per_slot, head_dim
    ).transpose(0, 2, 1, 3, 4)
    query_rows = query_rows.reshape(row_count, slot_count, per_row * heads_per_slot, head_dim)
    scores = jnp.einsum(
        "rsad,rskd->rsak", query_rows, key_part, preferred_element_type=jnp.float32
    ) / math.sqrt(head_dim)
    entry_ids = jnp.arange(cache_span + per_row)[None, None, None, :]
    token_ids = (jnp.arange(per_row * heads_per_slot) // heads_per_slot)[None, None, :, None]
    allowed = jnp.where(
        entry_ids < cache_span,
        entry_ids < cached_len[:, None, None, None],
        entry_ids - cache_span <= token_ids,
    )
    scores = jnp.where(allowed, scores, -jnp.inf)
    peak_score = jnp.max(scores, axis=-1, keepdims=True)
    raised = jnp.exp(scores - peak_score)
    weights = (raised / jnp.sum(raised, axis=-1, keepdims=True)).astype(jnp.bfloat16)
    attended = jnp.einsum(
        "rsak,rskd->rsad", weights, value_part, preferred_element_type=jnp.float32
    ).astype(jnp.bfloat16)
    attended = attended.reshape(row_count, slot_count, per_row, heads_per_slot, head_dim).transpose(
        0, 2, 1, 3, 4
    )
    attended = attended.reshape(token_count, feat_width)
    plain_output = lax.psum_scatter(
        jnp.dot(attended, out_weight, preferred_element_type=jnp.float32).astype(jnp.bfloat16),
        "tp",
        scatter_dimension=1,
        tiled=True,
    ).astype(jnp.float32)
    slot_hits = adapter_ids[:, None] == jnp.arange(pool_slot.shape[0])[None, :]
    pool_position = jnp.sum(jnp.where(slot_hits, pool_slot[None, :], 0), axis=1)
    replicas = lax.axis_size("rep")
    local_count = adapter_down.shape[0]
    capacity = (row_count + replicas - 1) // replicas + 1
    owner_of = pool_position // local_count
    local_slot = pool_position % local_count
    same_owner = owner_of[:, None] == owner_of[None, :]
    earlier = jnp.arange(row_count)[None, :] < jnp.arange(row_count)[:, None]
    seat_of = jnp.sum(same_owner & earlier, axis=1)
    target = owner_of * capacity + seat_of
    placing = jnp.arange(replicas * capacity)[:, None] == target[None, :]
    placing_mat = placing.astype(jnp.bfloat16)
    by_row = attended.reshape(row_count, per_row, feat_width)
    send_rows = jnp.einsum(
        "sr,rqf->sqf", placing_mat, by_row, preferred_element_type=jnp.float32
    ).astype(jnp.bfloat16)
    seat_slot = jnp.sum(jnp.where(placing, local_slot[None, :], 0), axis=1).astype(jnp.bfloat16)
    marker = jnp.broadcast_to(seat_slot[:, None, None], (replicas * capacity, 1, feat_width))
    payload = jnp.concatenate([send_rows, marker], axis=1).reshape(
        replicas, capacity, per_row + 1, feat_width
    )
    arrived = lax.all_to_all(payload, "rep", split_axis=0, concat_axis=0, tiled=True)
    arrived = arrived.reshape(replicas * capacity, per_row + 1, feat_width)
    seat_rows = arrived[:, :per_row, :]
    rank_size = adapter_down.shape[1]
    wants_one = arrived[:, per_row, :rank_size] > 0.5
    wants_one_out = arrived[:, per_row, :output_columns] > 0.5
    shrink_both = jnp.einsum(
        "sqf,jkf->jsqk", seat_rows, adapter_down, preferred_element_type=jnp.float32
    )
    shrink_part = jnp.where(wants_one[:, None, :], shrink_both[1], shrink_both[0])
    down_projected = tp_sum(shrink_part.astype(jnp.bfloat16))
    up_both = jnp.einsum(
        "sqk,jkd->jsqd", down_projected, pooled_up_weight, preferred_element_type=jnp.float32
    )
    seat_delta = jnp.where(wants_one_out[:, None, :], up_both[1], up_both[0]).astype(jnp.bfloat16)
    returned = lax.all_to_all(
        seat_delta.reshape(replicas, capacity, per_row, output_columns),
        "rep",
        split_axis=0,
        concat_axis=0,
        tiled=True,
    ).reshape(replicas * capacity, per_row, output_columns)
    adapter_correction = jnp.einsum(
        "sr,sqd->rqd", placing_mat, returned, preferred_element_type=jnp.float32
    )
    adapted_output = plain_output + ADAPTER_SCALE * adapter_correction.reshape(
        token_count, output_columns
    )
    return adapted_output.astype(jnp.bfloat16)


def solution(mesh):
    return jax.shard_map(
        shards,
        mesh=mesh,
        in_specs=(
            P("rep", "tp"),
            P("rep", "tp"),
            P("rep", "tp", None, None),
            P("rep"),
            P("rep", None),
            P("tp", None),
            P("rep", None, "tp"),
            P("rep", None, "tp"),
            P("rep"),
            P(),
        ),
        out_specs=P("rep", "tp"),
        check_vma=False,
    )
```

```python
import math

import jax
import jax.numpy as jnp
from jax import lax
from jax.sharding import PartitionSpec as P

ADAPTER_SCALE = 2.0


def tp_sum(part):
    width = lax.axis_size("tp")
    seats, tokens, rank = part.shape
    lanes = part.reshape(seats // 2, 2, tokens, rank).transpose(2, 0, 1, 3)
    lanes = lanes.reshape(tokens, seats // 2, 2 * rank)
    chunks = lanes.reshape(width, -1, 2 * rank)
    gathered = lax.all_to_all(chunks, "tp", split_axis=0, concat_axis=0, tiled=True)
    summed = jnp.sum(gathered.astype(jnp.float32), axis=0, keepdims=True).astype(jnp.bfloat16)
    spread = lax.all_to_all(
        jnp.broadcast_to(summed, chunks.shape), "tp", split_axis=0, concat_axis=0, tiled=True
    )
    spread = spread.reshape(tokens, seats // 2, 2, rank).transpose(1, 2, 0, 3)
    return spread.reshape(seats, tokens, rank)


def shards(
    queries,
    fresh_kv,
    kv_cache,
    cached_len,
    page_table,
    out_weight,
    adapter_down,
    pooled_up_weight,
    adapter_ids,
    pool_slot,
):
    row_count = cached_len.shape[0]
    token_count = queries.shape[0]
    per_row = token_count // row_count
    slot_count = kv_cache.shape[1]
    page_len = kv_cache.shape[2]
    head_dim = kv_cache.shape[3] // 2
    feat_width = queries.shape[1]
    head_count = feat_width // head_dim
    heads_per_slot = head_count // slot_count
    cache_span = page_table.shape[1] * page_len
    output_columns = pooled_up_weight.shape[2]
    paged_kv = (
        kv_cache[page_table]
        .transpose(0, 2, 1, 3, 4)
        .reshape(row_count, slot_count, cache_span, 2 * head_dim)
    )
    recent = fresh_kv.reshape(row_count, per_row, slot_count, 2 * head_dim).transpose(0, 2, 1, 3)
    entries = jnp.concatenate([paged_kv, recent], axis=2)
    key_part = entries[..., :head_dim]
    value_part = entries[..., head_dim:]
    query_rows = queries.reshape(
        row_count, per_row, slot_count, heads_per_slot, head_dim
    ).transpose(0, 2, 1, 3, 4)
    query_rows = query_rows.reshape(row_count, slot_count, per_row * heads_per_slot, head_dim)
    scores = jnp.einsum(
        "rsad,rskd->rsak", query_rows, key_part, preferred_element_type=jnp.float32
    ) / math.sqrt(head_dim)
    entry_ids = jnp.arange(cache_span + per_row)[None, None, None, :]
    token_ids = (jnp.arange(per_row * heads_per_slot) // heads_per_slot)[None, None, :, None]
    allowed = jnp.where(
        entry_ids < cache_span,
        entry_ids < cached_len[:, None, None, None],
        entry_ids - cache_span <= token_ids,
    )
    scores = jnp.where(allowed, scores, -jnp.inf)
    peak_score = jnp.max(scores, axis=-1, keepdims=True)
    raised = jnp.exp(scores - peak_score)
    weights = (raised / jnp.sum(raised, axis=-1, keepdims=True)).astype(jnp.bfloat16)
    attended = jnp.einsum(
        "rsak,rskd->rsad", weights, value_part, preferred_element_type=jnp.float32
    ).astype(jnp.bfloat16)
    attended = attended.reshape(row_count, slot_count, per_row, heads_per_slot, head_dim).transpose(
        0, 2, 1, 3, 4
    )
    attended = attended.reshape(token_count, feat_width)
    plain_output = lax.psum_scatter(
        jnp.dot(attended, out_weight, preferred_element_type=jnp.float32).astype(jnp.bfloat16),
        "tp",
        scatter_dimension=1,
        tiled=True,
    ).astype(jnp.float32)
    slot_hits = adapter_ids[:, None] == jnp.arange(pool_slot.shape[0])[None, :]
    pool_position = jnp.sum(jnp.where(slot_hits, pool_slot[None, :], 0), axis=1)
    replicas = lax.axis_size("rep")
    local_count = adapter_down.shape[0]
    capacity = (row_count + replicas - 1) // replicas + 1
    owner_of = pool_position // local_count
    local_slot = pool_position % local_count
    same_owner = owner_of[:, None] == owner_of[None, :]
    earlier = jnp.arange(row_count)[None, :] < jnp.arange(row_count)[:, None]
    seat_of = jnp.sum(same_owner & earlier, axis=1)
    target = owner_of * capacity + seat_of
    placing = jnp.arange(replicas * capacity)[:, None] == target[None, :]
    placing_mat = placing.astype(jnp.bfloat16)
    by_row = attended.reshape(row_count, per_row, feat_width)
    send_rows = jnp.einsum(
        "sr,rqf->sqf", placing_mat, by_row, preferred_element_type=jnp.float32
    ).astype(jnp.bfloat16)
    seat_slot = jnp.sum(jnp.where(placing, local_slot[None, :], 0), axis=1).astype(jnp.bfloat16)
    marker = jnp.broadcast_to(seat_slot[:, None, None], (replicas * capacity, 1, feat_width))
    payload = jnp.concatenate([send_rows, marker], axis=1).reshape(
        replicas, capacity, per_row + 1, feat_width
    )
    arrived = lax.all_to_all(payload, "rep", split_axis=0, concat_axis=0, tiled=True)
    arrived = arrived.reshape(replicas * capacity, per_row + 1, feat_width)
    seat_rows = arrived[:, :per_row, :]
    rank_size = adapter_down.shape[1]
    wants_one = arrived[:, per_row, :rank_size] > 0.5
    wants_one_out = arrived[:, per_row, :output_columns] > 0.5
    shrink_both = jnp.einsum(
        "sqf,jkf->jsqk", seat_rows, adapter_down, preferred_element_type=jnp.float32
    )
    shrink_part = jnp.where(wants_one[:, None, :], shrink_both[1], shrink_both[0])
    down_projected = tp_sum(shrink_part.astype(jnp.bfloat16))
    up_both = jnp.einsum(
        "sqk,jkd->jsqd", down_projected, pooled_up_weight, preferred_element_type=jnp.float32
    )
    seat_delta = jnp.where(wants_one_out[:, None, :], up_both[1], up_both[0]).astype(jnp.bfloat16)
    returned = lax.all_to_all(
        seat_delta.reshape(replicas, capacity, per_row, output_columns),
        "rep",
        split_axis=0,
        concat_axis=0,
        tiled=True,
    ).reshape(replicas * capacity, per_row, output_columns)
    adapter_correction = jnp.einsum(
        "sr,sqd->rqd", placing_mat, returned, preferred_element_type=jnp.float32
    )
    adapted_output = plain_output + ADAPTER_SCALE * adapter_correction.reshape(
        token_count, output_columns
    )
    return adapted_output.astype(jnp.bfloat16)


def solution(mesh):
    return jax.shard_map(
        shards,
        mesh=mesh,
        in_specs=(
            P("rep", "tp"),
            P("rep", "tp"),
            P("rep", "tp", None, None),
            P("rep"),
            P("rep", None),
            P("tp", None),
            P("rep", None, "tp"),
            P("rep", None, "tp"),
            P("rep"),
            P(),
        ),
        out_specs=P("rep", "tp"),
        check_vma=False,
    )
```
